128 devices in a mesh: loop: 16 (over x_hi, z, core), width: 8 (over x_lo, y).
Axes of the slice: x: 4 (x_hi: 2, x_lo: 2; x = x_hi * 2 + x_lo), y: 4, z: 4, core: 2. Of those that a mesh axis runs over, the one named last changes fastest.
Arguments:
- queries: bfloat16 [16384, 4096], P('loop', 'width'), may hold values from -0.0625 to 0.0625
- passages: bfloat16 [16384, 4096], P('loop', 'width'), may hold values from -0.0625 to 0.0625
- teacher: bfloat16 [16384, 4096], P('loop'), may hold values from -5 to 12
- positives: int32 [16384], P('loop'), may hold values from 0 to 4095
Outputs:
- grad_queries: float32 [16384, 4096], P('loop', 'width')
- grad_passages: float32 [16384, 4096], P('loop', 'width')
The draws below stay inside these ranges and needn't reach their ends.
All inputs are finite; a program needn't handle non-finite values.
Results may differ from the reference program's by a relative error of at most 0.0003.
Values may be sent and summed in bfloat16 or wider, within the bound.
No kernel may reach another device: no remote copies, remote signals or barrier semaphores. Data moves between devices by JAX's collectives and lax.ppermute only.
A program may use at most 192 MiB of HBM per device.

```python
import jax
import jax.numpy as jnp
from jax import lax

D = 4096
ROWS = 1024
STEPS = 4
NQ = 16384
WINDOW = 4096
N_LOOP = 16
N_WIDTH = 8


def cluster_plan(key):
    centre_count = 16
    block_count = NQ // ROWS
    passage_ids = jax.random.randint(jax.random.fold_in(key, 11), (NQ,), 0, centre_count, dtype=jnp.int32)
    chosen = jax.random.randint(jax.random.fold_in(key, 12), (NQ,), 0, WINDOW, dtype=jnp.int32)
    chosen = chosen.at[0].set(WINDOW - 1).at[1].set(0)
    rows_all = jnp.arange(NQ, dtype=jnp.int32)
    owner_row = (rows_all // ROWS - chosen // ROWS) % block_count * ROWS + chosen % ROWS
    query_ids = passage_ids[owner_row]
    return (passage_ids, query_ids, chosen)


def centre_rows(key):
    sign_bits = jax.random.bernoulli(jax.random.fold_in(key, 13), 0.5, (16, D))
    height = (0.5 / D) ** 0.5
    return jnp.where(sign_bits, height, -height).astype(jnp.float32)


def embed_rows(key, cluster_ids, salt):
    centres = centre_rows(key)
    noise_scale = (0.5 / D) ** 0.5
    full_shape = (NQ, D)
    spread = jax.random.truncated_normal(jax.random.fold_in(key, salt), -4.0, 4.0, full_shape, jnp.float32)
    return (centres[cluster_ids] + noise_scale * spread).astype(jnp.bfloat16)


def draw_queries(key, part):
    passage_ids, query_ids, chosen = cluster_plan(key)
    return embed_rows(key, query_ids, 21)


def draw_passages(key, part):
    passage_ids, query_ids, chosen = cluster_plan(key)
    return embed_rows(key, passage_ids, 22)


def draw_teacher(key, part):
    passage_ids, query_ids, chosen = cluster_plan(key)
    affinity = jax.random.uniform(jax.random.fold_in(key, 31), (16, 16), jnp.float32, -3.0, 3.0)
    jitter = 0.5 * jax.random.truncated_normal(jax.random.fold_in(key, 33), -3.0, 3.0, (NQ, WINDOW), jnp.float32)
    query_rows = jnp.arange(NQ, dtype=jnp.int32)[:, None]
    columns = jnp.arange(WINDOW, dtype=jnp.int32)[None, :]
    window_rows = (query_rows // ROWS - columns // ROWS) % (NQ // ROWS) * ROWS + columns % ROWS
    column_ids = passage_ids[window_rows]
    row_ids = jnp.broadcast_to(query_ids[:, None], column_ids.shape)
    same_group = row_ids == column_ids
    baseline = jnp.where(same_group, 10.0, affinity[row_ids, column_ids])
    return (baseline + jitter).astype(jnp.bfloat16)


def draw_positives(key, part):
    passage_ids, query_ids, chosen = cluster_plan(key)
    return chosen


def setup_inputs(seed: int = 0) -> dict:
    arg_keys = jax.random.split(jax.random.key(seed), 5)
    queries = draw_queries(jax.random.fold_in(arg_keys[4], 71), 0)
    passages = draw_passages(jax.random.fold_in(arg_keys[4], 71), 0)
    teacher = draw_teacher(jax.random.fold_in(arg_keys[4], 71), 0)
    positives = draw_positives(jax.random.fold_in(arg_keys[4], 71), 0)
    return dict(queries=queries, passages=passages, teacher=teacher, positives=positives)


SCALE = 20.0


def slopes_of(scores, teacher, positives):
    teach = teacher.astype(jnp.float32)
    index = positives[:, None].astype(jnp.int32)
    s_pos = jnp.take_along_axis(scores, index, 1)
    t_pos = jnp.take_along_axis(teach, index, 1)
    errors = (s_pos - scores) - (t_pos - teach)
    total = jnp.sum(errors, 1, keepdims=True)
    column = lax.broadcasted_iota(jnp.int32, scores.shape, 1)
    hit = (column == index).astype(jnp.float32)
    coef = SCALE * 2.0 / (scores.shape[1] - 1)
    return coef * (hit * total - errors)


def reference(queries, passages, teacher, positives):
    part_width = D // N_WIDTH
    blocks_q = queries.reshape(N_LOOP, ROWS, D)
    blocks_p = passages.reshape(N_LOOP, ROWS, D)
    blocks_t = teacher.reshape(N_LOOP, ROWS, WINDOW)
    blocks_pos = positives.reshape(N_LOOP, ROWS)
    offsets = jnp.arange(STEPS, dtype=jnp.int32)

    def one_block(carry, inputs):
        block, query, teach, posit = inputs
        owners = (block - offsets) % N_LOOP
        window = blocks_p[owners].reshape(WINDOW, D)
        total = jnp.zeros((ROWS, WINDOW), jnp.float32)
        for slot in range(N_WIDTH):
            lower = slot * part_width
            part = jnp.dot(query[:, lower:lower + part_width], window[:, lower:lower + part_width].T,
                           preferred_element_type=jnp.float32)
            total = total + part
        scores = SCALE * total
        slopes = slopes_of(scores, teach, posit)
        grad_q = jnp.dot(slopes, window.astype(jnp.float32), precision=lax.Precision.HIGHEST,
                         preferred_element_type=jnp.float32)
        terms = jnp.dot(slopes.T, query.astype(jnp.float32), precision=lax.Precision.HIGHEST,
                        preferred_element_type=jnp.float32)
        carry = carry.at[owners].add(terms.reshape(STEPS, ROWS, D))
        return carry, grad_q

    start = jnp.zeros((N_LOOP, ROWS, D), jnp.float32)
    blocks = jnp.arange(N_LOOP, dtype=jnp.int32)
    grad_p, grad_q = lax.scan(one_block, start, (blocks, blocks_q, blocks_t, blocks_pos))
    return grad_q.reshape(NQ, D), grad_p.reshape(NQ, D)
```

```python
import jax
import jax.numpy as jnp
from jax import lax
from jax.sharding import PartitionSpec as P

STEPS = 4


SCALE = 20.0


def shifted(block, axis, distance):
    devices = range(lax.axis_size(axis))
    route = [((i - distance) % len(devices), i) for i in devices]
    return lax.ppermute(block, axis, route)


def after(value, dep):
    return value + 0.0 * dep[:1, :1]


def per_device(queries, passages, teacher, positives):
    rows = queries.shape[0]
    window = STEPS * rows
    held = [passages]
    current = passages
    for step in range(1, STEPS):
        current = shifted(current, "loop", 1)
        held.append(current)

    index = positives[:, None]
    teach = teacher.astype(jnp.float32)
    column = lax.broadcasted_iota(jnp.int32, teach.shape, 1)
    t_pos = jnp.sum(jnp.where(column == index, teach, 0.0), 1, keepdims=True)
    t_sum = jnp.sum(teach, 1, keepdims=True)

    partials = [
        jnp.einsum("qd,pd->qp", queries, block, preferred_element_type=jnp.float32)
        for block in held
    ]
    block_col = lax.broadcasted_iota(jnp.int32, (rows, rows), 1)
    pos_part = sum(
        jnp.sum(jnp.where(block_col + k * rows == index, partials[k], 0.0), 1)
        for k in range(STEPS)
    )
    row_part = sum(jnp.sum(partials[k], 1) for k in range(STEPS))
    stats_part = jnp.stack([pos_part, row_part], 0)

    order = [0] + list(range(STEPS - 1, 0, -1))
    coef = SCALE * 2.0 / (window - 1)
    query_wide = queries.astype(jnp.float32)
    full = {}
    terms = {}
    grad_q = None
    grad_p = None

    def reduce_block(j):
        k = order[j]
        if j == 0:
            pad = jnp.zeros((8 - stats_part.shape[0], rows), jnp.float32)
            part = jnp.concatenate([partials[k], stats_part, pad], 0)
            carried = lax.psum(part, "width")
            full[k] = carried[:rows]
            return carried[rows : rows + stats_part.shape[0]]
        part = after(partials[k], full[order[j - 1]])
        if j >= 2:
            part = after(part, terms[order[j - 2]])
        full[k] = lax.psum(part, "width")
        return None

    stats = reduce_block(0)
    s_pos = SCALE * stats[0][:, None]
    s_sum = SCALE * stats[1][:, None]
    total = window * (s_pos - t_pos) - s_sum + t_sum

    for j, k in enumerate(order):
        if j + 1 < len(order):
            reduce_block(j + 1)
        scores = SCALE * full[k]
        teach_k = teach[:, k * rows : (k + 1) * rows]
        errors = (s_pos - scores) - (t_pos - teach_k)
        hit = (block_col + k * rows == index).astype(jnp.float32)
        slopes = coef * (hit * total - errors)
        gq = jnp.dot(
            slopes,
            held[k].astype(jnp.float32),
            precision=lax.Precision.HIGHEST,
            preferred_element_type=jnp.float32,
        )
        grad_q = gq if grad_q is None else grad_q + gq
        term = jnp.dot(
            slopes.T,
            query_wide,
            precision=lax.Precision.HIGHEST,
            preferred_element_type=jnp.float32,
        )
        terms[k] = term
        if k:
            term = shifted(term, "loop", -k)
        grad_p = term if grad_p is None else grad_p + term
    return (grad_q, grad_p)


def solution(mesh):
    in_specs = (P("loop", "width"), P("loop", "width"), P("loop", None), P("loop"))
    out_specs = (P("loop", "width"), P("loop", "width"))
    return jax.shard_map(
        per_device, mesh=mesh, in_specs=in_specs, out_specs=out_specs, check_vma=False
    )
```

```python
import jax
import jax.numpy as jnp
from jax import lax
from jax.sharding import PartitionSpec as P

STEPS = 4


SCALE = 20.0


def shifted(block, axis, distance):
    devices = range(lax.axis_size(axis))
    route = [((i - distance) % len(devices), i) for i in devices]
    return lax.ppermute(block, axis, route)


def wide_dot(a, b):
    return jnp.dot(a, b, precision=lax.Precision.HIGHEST, preferred_element_type=jnp.float32)


def per_device(queries, passages, teacher, positives):
    rows = queries.shape[0]
    width = lax.axis_size("width")
    me = lax.axis_index("width")
    sub = rows // width
    window = STEPS * rows

    q_full = lax.all_gather(queries, "width", axis=1, tiled=True)
    p_cols = lax.all_to_all(passages, "width", 0, 1, tiled=True)
    held_cols = [p_cols]
    held = [passages]
    for step in range(1, STEPS):
        held_cols.append(shifted(held_cols[-1], "loop", 1))
        held.append(shifted(held[-1], "loop", 1))

    cols = jnp.concatenate(held_cols, 0)
    scores = SCALE * jnp.einsum("qd,cd->qc", q_full, cols, preferred_element_type=jnp.float32)

    index = positives[:, None]
    teach = teacher.astype(jnp.float32)
    column = lax.broadcasted_iota(jnp.int32, teach.shape, 1)
    t_pos = jnp.sum(jnp.where(column == index, teach, 0.0), 1, keepdims=True)
    t_sum = jnp.sum(teach, 1, keepdims=True)

    local = lax.broadcasted_iota(jnp.int32, (1, STEPS * sub), 1)
    wcol = (local // sub) * rows + me * sub + local % sub
    hit = wcol == index
    teach_cols = lax.dynamic_slice_in_dim(
        teach.reshape(rows, STEPS, width, sub), me, 1, 2
    ).reshape(rows, STEPS * sub)

    pos_part = jnp.sum(jnp.where(hit, scores, 0.0), 1)
    row_part = jnp.sum(scores, 1)
    stats = lax.psum(jnp.stack([pos_part, row_part], 0), "width")
    s_pos = stats[0][:, None]
    s_sum = stats[1][:, None]
    total = window * (s_pos - t_pos) - s_sum + t_sum
    coef = SCALE * 2.0 / (window - 1)
    errors = (s_pos - scores) - (t_pos - teach_cols)
    slopes_cols = coef * (hit.astype(jnp.float32) * total - errors)

    slopes = lax.all_gather(slopes_cols, "width", axis=1, tiled=True)
    slopes = slopes.reshape(rows, width, STEPS, sub)

    query_wide = queries.astype(jnp.float32)
    grad_q = None
    terms = []
    for k in range(STEPS):
        block_slopes = slopes[:, :, k, :].reshape(rows, rows)
        gq = wide_dot(block_slopes, held[k].astype(jnp.float32))
        grad_q = gq if grad_q is None else grad_q + gq
        terms.append(wide_dot(block_slopes.T, query_wide))
    grad_p = terms[STEPS - 1]
    for k in range(STEPS - 2, -1, -1):
        grad_p = shifted(grad_p, "loop", -1) + terms[k]
    return (grad_q, grad_p)


def solution(mesh):
    in_specs = (P("loop", "width"), P("loop", "width"), P("loop", None), P("loop"))
    out_specs = (P("loop", "width"), P("loop", "width"))
    return jax.shard_map(
        per_device, mesh=mesh, in_specs=in_specs, out_specs=out_specs, check_vma=False
    )
```

```python
import jax
import jax.numpy as jnp
from jax import lax
from jax.sharding import PartitionSpec as P

STEPS = 4


SCALE = 20.0


def shifted(block, axis, distance):
    devices = range(lax.axis_size(axis))
    route = [((i - distance) % len(devices), i) for i in devices]
    return lax.ppermute(block, axis, route)


def after(value, dep):
    zero = 0.0 * dep[:1, :1]
    return value + zero.astype(value.dtype)


def wide_dot(a, b):
    return jnp.dot(a, b, precision=lax.Precision.HIGHEST, preferred_element_type=jnp.float32)


def per_device(queries, passages, teacher, positives):
    rows = queries.shape[0]
    width = lax.axis_size("width")
    me = lax.axis_index("width")
    sub = rows // width
    window = STEPS * rows

    q_full = lax.all_gather(queries, "width", axis=1, tiled=True)
    p_cols = lax.all_to_all(passages, "width", 0, 1, tiled=True)
    held_cols = [p_cols]
    for step in range(1, STEPS):
        held_cols.append(shifted(held_cols[-1], "loop", 1))

    cols = jnp.concatenate(held_cols, 0)
    scores = SCALE * jnp.einsum("qd,cd->qc", q_full, cols, preferred_element_type=jnp.float32)

    index = positives[:, None]
    teach = teacher.astype(jnp.float32)
    column = lax.broadcasted_iota(jnp.int32, teach.shape, 1)
    t_pos = jnp.sum(jnp.where(column == index, teach, 0.0), 1, keepdims=True)
    t_sum = jnp.sum(teach, 1, keepdims=True)

    local = lax.broadcasted_iota(jnp.int32, (1, STEPS * sub), 1)
    wcol = (local // sub) * rows + me * sub + local % sub
    hit = wcol == index
    teach_cols = lax.dynamic_slice_in_dim(
        teach.reshape(rows, STEPS, width, sub), me, 1, 2
    ).reshape(rows, STEPS * sub)

    pos_part = jnp.sum(jnp.where(hit, scores, 0.0), 1)
    row_part = jnp.sum(scores, 1)
    stats = lax.psum(jnp.stack([pos_part, row_part], 0), "width")
    s_pos = stats[0][:, None]
    s_sum = stats[1][:, None]
    total = window * (s_pos - t_pos) - s_sum + t_sum
    coef = SCALE * 2.0 / (window - 1)
    errors = (s_pos - scores) - (t_pos - teach_cols)
    slopes_cols = coef * (hit.astype(jnp.float32) * total - errors)

    held = [after(passages, stats)]
    for step in range(1, STEPS):
        held.append(shifted(held[-1], "loop", 1))

    query_wide = queries.astype(jnp.float32)
    grad_q = None
    grad_p = None
    done = []
    for j, k in enumerate(range(STEPS - 1, -1, -1)):
        piece = slopes_cols[:, k * sub : (k + 1) * sub]
        if j >= 1:
            piece = after(piece, done[j - 1][0])
        if j >= 2:
            piece = after(after(piece, done[j - 2][1]), held[STEPS - 1])
        block_slopes = lax.all_gather(piece, "width", axis=1, tiled=True)
        gq = wide_dot(block_slopes, held[k].astype(jnp.float32))
        grad_q = gq if grad_q is None else grad_q + gq
        term = wide_dot(block_slopes.T, query_wide)
        grad_p = term if grad_p is None else shifted(grad_p, "loop", -1) + term
        done.append((block_slopes, grad_p))
    return (grad_q, grad_p)


def solution(mesh):
    in_specs = (P("loop", "width"), P("loop", "width"), P("loop", None), P("loop"))
    out_specs = (P("loop", "width"), P("loop", "width"))
    return jax.shard_map(
        per_device, mesh=mesh, in_specs=in_specs, out_specs=out_specs, check_vma=False
    )
```

```python
import jax
import jax.numpy as jnp
from jax import lax
from jax.sharding import PartitionSpec as P

STEPS = 4


SCALE = 20.0


def shifted(block, axis, distance):
    devices = range(lax.axis_size(axis))
    route = [((i - distance) % len(devices), i) for i in devices]
    return lax.ppermute(block, axis, route)


def wide_dot(a, b):
    return jnp.dot(a, b, precision=lax.Precision.HIGHEST, preferred_element_type=jnp.float32)


def per_device(queries, passages, teacher, positives):
    rows = queries.shape[0]
    width = lax.axis_size("width")
    me = lax.axis_index("width")
    sub = rows // width
    window = STEPS * rows

    q_full = lax.all_gather(queries, "width", axis=1, tiled=True)
    held = [passages]
    for step in range(1, STEPS):
        held.append(shifted(held[-1], "loop", 1))
    held_cols = [lax.all_to_all(block, "width", 0, 1, tiled=True) for block in held]

    cols = jnp.concatenate(held_cols, 0)
    scores = SCALE * jnp.einsum("qd,cd->qc", q_full, cols, preferred_element_type=jnp.float32)

    index = positives[:, None]
    teach = teacher.astype(jnp.float32)
    column = lax.broadcasted_iota(jnp.int32, teach.shape, 1)
    t_pos = jnp.sum(jnp.where(column == index, teach, 0.0), 1, keepdims=True)
    t_sum = jnp.sum(teach, 1, keepdims=True)

    local = lax.broadcasted_iota(jnp.int32, (1, STEPS * sub), 1)
    wcol = (local // sub) * rows + me * sub + local % sub
    hit = wcol == index
    teach_cols = lax.dynamic_slice_in_dim(
        teach.reshape(rows, STEPS, width, sub), me, 1, 2
    ).reshape(rows, STEPS * sub)

    pos_part = jnp.sum(jnp.where(hit, scores, 0.0), 1)
    row_part = jnp.sum(scores, 1)
    stats = lax.psum(jnp.stack([pos_part, row_part], 0), "width")
    s_pos = stats[0][:, None]
    s_sum = stats[1][:, None]
    total = window * (s_pos - t_pos) - s_sum + t_sum
    coef = SCALE * 2.0 / (window - 1)
    errors = (s_pos - scores) - (t_pos - teach_cols)
    slopes_cols = coef * (hit.astype(jnp.float32) * total - errors)

    slopes = lax.all_gather(slopes_cols, "width", axis=1, tiled=True)
    slopes = slopes.reshape(rows, width, STEPS, sub)

    query_wide = queries.astype(jnp.float32)
    grad_q = None
    terms = []
    for k in range(STEPS):
        block_slopes = slopes[:, :, k, :].reshape(rows, rows)
        gq = wide_dot(block_slopes, held[k].astype(jnp.float32))
        grad_q = gq if grad_q is None else grad_q + gq
        terms.append(wide_dot(block_slopes.T, query_wide))
    grad_p = terms[STEPS - 1]
    for k in range(STEPS - 2, -1, -1):
        grad_p = shifted(grad_p, "loop", -1) + terms[k]
    return (grad_q, grad_p)


def solution(mesh):
    in_specs = (P("loop", "width"), P("loop", "width"), P("loop", None), P("loop"))
    out_specs = (P("loop", "width"), P("loop", "width"))
    return jax.shard_map(
        per_device, mesh=mesh, in_specs=in_specs, out_specs=out_specs, check_vma=False
    )
```

```python
import jax
import jax.numpy as jnp
from jax import lax
from jax.sharding import PartitionSpec as P

STEPS = 4


SCALE = 20.0


def shifted(block, axis, distance):
    devices = range(lax.axis_size(axis))
    route = [((i - distance) % len(devices), i) for i in devices]
    return lax.ppermute(block, axis, route)


def wide_dot(a, b):
    return jnp.dot(a, b, precision=lax.Precision.HIGHEST, preferred_element_type=jnp.float32)


def per_device(queries, passages, teacher, positives):
    rows = queries.shape[0]
    width = lax.axis_size("width")
    me = lax.axis_index("width")
    sub = rows // width
    window = STEPS * rows

    q_full = lax.all_gather(queries, "width", axis=1, tiled=True)
    p_cols = lax.all_to_all(passages, "width", 0, 1, tiled=True)
    held_cols = [p_cols]
    held = [passages]
    for step in range(1, STEPS):
        held_cols.append(shifted(held_cols[-1], "loop", 1))
        held.append(shifted(held[-1], "loop", 1))

    cols = jnp.concatenate(held_cols, 0)
    raw = jnp.einsum("qd,cd->qc", q_full, cols, preferred_element_type=jnp.float32)
    scores = SCALE * lax.all_gather(raw, "width", axis=1, tiled=True)

    index = positives[:, None]
    teach = teacher.astype(jnp.float32)
    column = lax.broadcasted_iota(jnp.int32, teach.shape, 1)
    t_pos = jnp.sum(jnp.where(column == index, teach, 0.0), 1, keepdims=True)
    teach_perm = (
        teach.reshape(rows, STEPS, width, sub).transpose(0, 2, 1, 3).reshape(rows, window)
    )
    place = lax.broadcasted_iota(jnp.int32, (1, window), 1)
    wcol = ((place // sub) % STEPS) * rows + (place // (STEPS * sub)) * sub + place % sub
    hit = wcol == index
    s_pos = jnp.sum(jnp.where(hit, scores, 0.0), 1, keepdims=True)
    errors = (s_pos - scores) - (t_pos - teach_perm)
    total = jnp.sum(errors, 1, keepdims=True)
    coef = SCALE * 2.0 / (window - 1)
    slopes = coef * (hit.astype(jnp.float32) * total - errors)
    slopes = slopes.reshape(rows, width, STEPS, sub)

    query_wide = queries.astype(jnp.float32)
    grad_q = None
    terms = []
    for k in range(STEPS):
        block_slopes = slopes[:, :, k, :].reshape(rows, rows)
        gq = wide_dot(block_slopes, held[k].astype(jnp.float32))
        grad_q = gq if grad_q is None else grad_q + gq
        terms.append(wide_dot(block_slopes.T, query_wide))
    grad_p = terms[STEPS - 1]
    for k in range(STEPS - 2, -1, -1):
        grad_p = shifted(grad_p, "loop", -1) + terms[k]
    return (grad_q, grad_p)


def solution(mesh):
    in_specs = (P("loop", "width"), P("loop", "width"), P("loop", None), P("loop"))
    out_specs = (P("loop", "width"), P("loop", "width"))
    return jax.shard_map(
        per_device, mesh=mesh, in_specs=in_specs, out_specs=out_specs, check_vma=False
    )
```

```python
import jax
import jax.numpy as jnp
from jax import lax
from jax.sharding import PartitionSpec as P

STEPS = 4


SCALE = 20.0


def shifted(block, axis, distance):
    devices = range(lax.axis_size(axis))
    route = [((i - distance) % len(devices), i) for i in devices]
    return lax.ppermute(block, axis, route)


def after(value, dep):
    zero = 0.0 * dep[:1, :1]
    return value + zero.astype(value.dtype)


def wide_dot(a, b):
    return jnp.dot(a, b, precision=lax.Precision.HIGHEST, preferred_element_type=jnp.float32)


def per_device(queries, passages, teacher, positives):
    rows = queries.shape[0]
    width = lax.axis_size("width")
    me = lax.axis_index("width")
    sub = rows // width
    window = STEPS * rows

    q_full = lax.all_gather(queries, "width", axis=1, tiled=True)
    p_cols = lax.all_to_all(passages, "width", 0, 1, tiled=True)
    held_cols = [p_cols]
    for step in range(1, STEPS):
        held_cols.append(shifted(held_cols[-1], "loop", 1))
    held = [passages]
    current = after(passages, q_full)
    for step in range(1, STEPS):
        current = shifted(current, "loop", 1)
        held.append(current)

    cols = jnp.concatenate(held_cols, 0)
    scores = SCALE * jnp.einsum("qd,cd->qc", q_full, cols, preferred_element_type=jnp.float32)

    index = positives[:, None]
    teach = teacher.astype(jnp.float32)
    column = lax.broadcasted_iota(jnp.int32, teach.shape, 1)
    t_pos = jnp.sum(jnp.where(column == index, teach, 0.0), 1, keepdims=True)
    t_sum = jnp.sum(teach, 1, keepdims=True)

    local = lax.broadcasted_iota(jnp.int32, (1, STEPS * sub), 1)
    wcol = (local // sub) * rows + me * sub + local % sub
    hit = wcol == index
    teach_cols = lax.dynamic_slice_in_dim(
        teach.reshape(rows, STEPS, width, sub), me, 1, 2
    ).reshape(rows, STEPS * sub)

    pos_part = jnp.sum(jnp.where(hit, scores, 0.0), 1)
    row_part = jnp.sum(scores, 1)
    stats = lax.psum(jnp.stack([pos_part, row_part], 0), "width")
    s_pos = stats[0][:, None]
    s_sum = stats[1][:, None]
    total = window * (s_pos - t_pos) - s_sum + t_sum
    coef = SCALE * 2.0 / (window - 1)
    errors = (s_pos - scores) - (t_pos - teach_cols)
    slopes_cols = coef * (hit.astype(jnp.float32) * total - errors)

    slopes = lax.all_gather(after(slopes_cols, held[-1]), "width", axis=1, tiled=True)
    slopes = slopes.reshape(rows, width, STEPS, sub)

    query_wide = queries.astype(jnp.float32)
    grad_q = None
    terms = []
    for k in range(STEPS):
        block_slopes = slopes[:, :, k, :].reshape(rows, rows)
        gq = wide_dot(block_slopes, held[k].astype(jnp.float32))
        grad_q = gq if grad_q is None else grad_q + gq
        terms.append(wide_dot(block_slopes.T, query_wide))
    grad_p = terms[STEPS - 1]
    for k in range(STEPS - 2, -1, -1):
        grad_p = shifted(grad_p, "loop", -1) + terms[k]
    return (grad_q, grad_p)


def solution(mesh):
    in_specs = (P("loop", "width"), P("loop", "width"), P("loop", None), P("loop"))
    out_specs = (P("loop", "width"), P("loop", "width"))
    return jax.shard_map(
        per_device, mesh=mesh, in_specs=in_specs, out_specs=out_specs, check_vma=False
    )
```

```python
import jax
import jax.numpy as jnp
from jax import lax
from jax.sharding import PartitionSpec as P

STEPS = 4


SCALE = 20.0


def shifted(block, axis, distance):
    devices = range(lax.axis_size(axis))
    route = [((i - distance) % len(devices), i) for i in devices]
    return lax.ppermute(block, axis, route)


def after(value, dep):
    zero = 0.0 * dep[:1, :1]
    return value + zero.astype(value.dtype)


def wide_dot(a, b):
    return jnp.dot(a, b, precision=lax.Precision.HIGHEST, preferred_element_type=jnp.float32)


def per_device(queries, passages, teacher, positives):
    rows = queries.shape[0]
    width = lax.axis_size("width")
    me = lax.axis_index("width")
    sub = rows // width
    window = STEPS * rows

    q_full = lax.all_gather(queries, "width", axis=1, tiled=True)
    p_cols = lax.all_to_all(passages, "width", 0, 1, tiled=True)
    held_cols = [p_cols]
    held = [passages]
    for step in range(1, STEPS):
        held_cols.append(shifted(held_cols[-1], "loop", 1))
        held.append(shifted(held[-1], "loop", 1))

    cols = jnp.concatenate(held_cols, 0)
    scores = SCALE * jnp.einsum("qd,cd->qc", q_full, cols, preferred_element_type=jnp.float32)

    index = positives[:, None]
    teach = teacher.astype(jnp.float32)
    column = lax.broadcasted_iota(jnp.int32, teach.shape, 1)
    t_pos = jnp.sum(jnp.where(column == index, teach, 0.0), 1, keepdims=True)
    t_sum = jnp.sum(teach, 1, keepdims=True)

    local = lax.broadcasted_iota(jnp.int32, (1, STEPS * sub), 1)
    wcol = (local // sub) * rows + me * sub + local % sub
    hit = wcol == index
    teach_cols = lax.dynamic_slice_in_dim(
        teach.reshape(rows, STEPS, width, sub), me, 1, 2
    ).reshape(rows, STEPS * sub)

    pos_part = jnp.sum(jnp.where(hit, scores, 0.0), 1)
    row_part = jnp.sum(scores, 1)
    stats = lax.psum(jnp.stack([pos_part, row_part], 0), "width")
    s_pos = stats[0][:, None]
    s_sum = stats[1][:, None]
    total = window * (s_pos - t_pos) - s_sum + t_sum
    coef = SCALE * 2.0 / (window - 1)
    errors = (s_pos - scores) - (t_pos - teach_cols)
    slopes_cols = coef * (hit.astype(jnp.float32) * total - errors)

    slopes = lax.all_gather(slopes_cols, "width", axis=1, tiled=True)
    slopes = slopes.reshape(rows, width, STEPS, sub)

    query_wide = queries.astype(jnp.float32)
    grad_q = None
    terms = []
    for k in range(STEPS):
        block_slopes = slopes[:, :, k, :].reshape(rows, rows)
        gq = wide_dot(block_slopes, held[k].astype(jnp.float32))
        grad_q = gq if grad_q is None else grad_q + gq
        terms.append(wide_dot(block_slopes.T, query_wide))
    half = terms[0].shape[1] // 2
    lead = terms[STEPS - 1][:, :half]
    trail = terms[STEPS - 1][:, half:]
    for k in range(STEPS - 2, -1, -1):
        lead = shifted(lead, "loop", -1)
        trail = shifted(after(trail, lead), "loop", -1)
        lead = lead + terms[k][:, :half]
        trail = trail + terms[k][:, half:]
    grad_p = jnp.concatenate([lead, trail], 1)
    return (grad_q, grad_p)


def solution(mesh):
    in_specs = (P("loop", "width"), P("loop", "width"), P("loop", None), P("loop"))
    out_specs = (P("loop", "width"), P("loop", "width"))
    return jax.shard_map(
        per_device, mesh=mesh, in_specs=in_specs, out_specs=out_specs, check_vma=False
    )
```

```python
import jax
import jax.numpy as jnp
from jax import lax
from jax.sharding import PartitionSpec as P

STEPS = 4


SCALE = 20.0


def shifted(block, axis, distance):
    devices = range(lax.axis_size(axis))
    route = [((i - distance) % len(devices), i) for i in devices]
    return lax.ppermute(block, axis, route)


def wide_dot(a, b):
    return jnp.dot(a, b, precision=lax.Precision.HIGHEST, preferred_element_type=jnp.float32)


def per_device(queries, passages, teacher, positives):
    rows = queries.shape[0]
    width = lax.axis_size("width")
    me = lax.axis_index("width")
    sub = rows // width
    window = STEPS * rows

    q_full = lax.all_gather(queries, "width", axis=1, tiled=True)
    p_cols = lax.all_to_all(passages, "width", 0, 1, tiled=True)
    held_cols = [p_cols]
    held = [passages]
    for step in range(1, STEPS):
        held_cols.append(shifted(held_cols[-1], "loop", 1))
        held.append(shifted(held[-1], "loop", 1))

    cols = jnp.concatenate(held_cols, 0)
    raw = jnp.einsum("qd,cd->qc", q_full, cols, preferred_element_type=jnp.float32)
    gathered = lax.all_gather(raw, "width", axis=1, tiled=True)
    gathered = gathered.reshape(rows, width, STEPS, sub)
    scores = SCALE * raw

    index = positives[:, None]
    teach = teacher.astype(jnp.float32)
    column = lax.broadcasted_iota(jnp.int32, teach.shape, 1)
    t_pos = jnp.sum(jnp.where(column == index, teach, 0.0), 1, keepdims=True)
    t_sum = jnp.sum(teach, 1, keepdims=True)

    local = lax.broadcasted_iota(jnp.int32, (1, STEPS * sub), 1)
    wcol = (local // sub) * rows + me * sub + local % sub
    hit = wcol == index
    teach_cols = lax.dynamic_slice_in_dim(
        teach.reshape(rows, STEPS, width, sub), me, 1, 2
    ).reshape(rows, STEPS * sub)

    pos_part = jnp.sum(jnp.where(hit, scores, 0.0), 1)
    row_part = jnp.sum(scores, 1) - jnp.sum(teach_cols, 1)
    stats = lax.psum(jnp.stack([pos_part, row_part], 0), "width")
    s_pos = stats[0][:, None]
    total = window * (s_pos - t_pos) - stats[1][:, None]
    coef = SCALE * 2.0 / (window - 1)
    block_col = lax.broadcasted_iota(jnp.int32, (rows, rows), 1)

    query_wide = queries.astype(jnp.float32)
    grad_q = None
    terms = []
    for k in range(STEPS):
        block_scores = SCALE * gathered[:, :, k, :].reshape(rows, rows)
        errors = (s_pos - block_scores) - (t_pos - teach[:, k * rows : (k + 1) * rows])
        block_hit = (block_col + k * rows == index).astype(jnp.float32)
        block_slopes = coef * (block_hit * total - errors)
        gq = wide_dot(block_slopes, held[k].astype(jnp.float32))
        grad_q = gq if grad_q is None else grad_q + gq
        terms.append(wide_dot(block_slopes.T, query_wide))
    grad_p = terms[STEPS - 1]
    for k in range(STEPS - 2, -1, -1):
        grad_p = shifted(grad_p, "loop", -1) + terms[k]
    return (grad_q, grad_p)


def solution(mesh):
    in_specs = (P("loop", "width"), P("loop", "width"), P("loop", None), P("loop"))
    out_specs = (P("loop", "width"), P("loop", "width"))
    return jax.shard_map(
        per_device, mesh=mesh, in_specs=in_specs, out_specs=out_specs, check_vma=False
    )
```

```python
import jax
import jax.numpy as jnp
from jax import lax
from jax.sharding import PartitionSpec as P

STEPS = 4


SCALE = 20.0


def shifted(block, axis, distance):
    devices = range(lax.axis_size(axis))
    route = [((i - distance) % len(devices), i) for i in devices]
    return lax.ppermute(block, axis, route)


def wide_dot(a, b):
    return jnp.dot(a, b, precision=lax.Precision.HIGH, preferred_element_type=jnp.float32)


def per_device(queries, passages, teacher, positives):
    rows = queries.shape[0]
    width = lax.axis_size("width")
    me = lax.axis_index("width")
    sub = rows // width
    window = STEPS * rows

    q_full = lax.all_gather(queries, "width", axis=1, tiled=True)
    p_cols = lax.all_to_all(passages, "width", 0, 1, tiled=True)
    held_cols = [p_cols]
    held = [passages]
    for step in range(1, STEPS):
        held_cols.append(shifted(held_cols[-1], "loop", 1))
        held.append(shifted(held[-1], "loop", 1))

    cols = jnp.concatenate(held_cols, 0)
    scores = SCALE * jnp.einsum("qd,cd->qc", q_full, cols, preferred_element_type=jnp.float32)

    index = positives[:, None]
    teach = teacher.astype(jnp.float32)
    column = lax.broadcasted_iota(jnp.int32, teach.shape, 1)
    t_pos = jnp.sum(jnp.where(column == index, teach, 0.0), 1, keepdims=True)
    t_sum = jnp.sum(teach, 1, keepdims=True)

    local = lax.broadcasted_iota(jnp.int32, (1, STEPS * sub), 1)
    wcol = (local // sub) * rows + me * sub + local % sub
    hit = wcol == index
    teach_cols = lax.dynamic_slice_in_dim(
        teach.reshape(rows, STEPS, width, sub), me, 1, 2
    ).reshape(rows, STEPS * sub)

    pos_part = jnp.sum(jnp.where(hit, scores, 0.0), 1)
    row_part = jnp.sum(scores, 1)
    stats = lax.psum(jnp.stack([pos_part, row_part], 0), "width")
    s_pos = stats[0][:, None]
    s_sum = stats[1][:, None]
    total = window * (s_pos - t_pos) - s_sum + t_sum
    coef = SCALE * 2.0 / (window - 1)
    errors = (s_pos - scores) - (t_pos - teach_cols)
    slopes_cols = coef * (hit.astype(jnp.float32) * total - errors)

    slopes = lax.all_gather(slopes_cols, "width", axis=1, tiled=True)
    slopes = slopes.reshape(rows, width, STEPS, sub)

    query_wide = queries.astype(jnp.float32)
    grad_q = None
    terms = []
    for k in range(STEPS):
        block_slopes = slopes[:, :, k, :].reshape(rows, rows)
        gq = wide_dot(block_slopes, held[k].astype(jnp.float32))
        grad_q = gq if grad_q is None else grad_q + gq
        terms.append(wide_dot(block_slopes.T, query_wide))
    grad_p = terms[STEPS - 1]
    for k in range(STEPS - 2, -1, -1):
        grad_p = shifted(grad_p, "loop", -1) + terms[k]
    return (grad_q, grad_p)


def solution(mesh):
    in_specs = (P("loop", "width"), P("loop", "width"), P("loop", None), P("loop"))
    out_specs = (P("loop", "width"), P("loop", "width"))
    return jax.shard_map(
        per_device, mesh=mesh, in_specs=in_specs, out_specs=out_specs, check_vma=False
    )
```

```python
import jax
import jax.numpy as jnp
from jax import lax
from jax.sharding import PartitionSpec as P

STEPS = 4


SCALE = 20.0


def shifted(block, axis, distance):
    devices = range(lax.axis_size(axis))
    route = [((i - distance) % len(devices), i) for i in devices]
    return lax.ppermute(block, axis, route)


def wide_dot(a, b):
    return jnp.dot(a, b, precision=lax.Precision.HIGH, preferred_element_type=jnp.float32)


def per_device(queries, passages, teacher, positives):
    rows = queries.shape[0]
    width = lax.axis_size("width")
    me = lax.axis_index("width")
    sub = rows // width
    window = STEPS * rows

    q_full = lax.all_gather(queries, "width", axis=1, tiled=True)
    p_cols = lax.all_to_all(passages, "width", 0, 1, tiled=True)
    held_cols = [p_cols]
    held = [passages]
    for step in range(1, STEPS):
        held_cols.append(shifted(held_cols[-1], "loop", 1))
        held.append(shifted(held[-1], "loop", 1))

    cols = jnp.concatenate(held_cols, 0)
    scores = SCALE * jnp.einsum("qd,cd->qc", q_full, cols, preferred_element_type=jnp.float32)

    index = positives[:, None]
    teach = teacher.astype(jnp.float32)
    column = lax.broadcasted_iota(jnp.int32, teach.shape, 1)
    t_pos = jnp.sum(jnp.where(column == index, teach, 0.0), 1, keepdims=True)
    t_sum = jnp.sum(teach, 1, keepdims=True)

    local = lax.broadcasted_iota(jnp.int32, (1, STEPS * sub), 1)
    wcol = (local // sub) * rows + me * sub + local % sub
    hit = wcol == index
    teach_cols = lax.dynamic_slice_in_dim(
        teach.reshape(rows, STEPS, width, sub), me, 1, 2
    ).reshape(rows, STEPS * sub)

    pos_part = jnp.sum(jnp.where(hit, scores, 0.0), 1)
    row_part = jnp.sum(scores, 1)
    stats = lax.psum(jnp.stack([pos_part, row_part], 0), "width")
    s_pos = stats[0][:, None]
    s_sum = stats[1][:, None]
    total = window * (s_pos - t_pos) - s_sum + t_sum
    coef = SCALE * 2.0 / (window - 1)
    errors = (s_pos - scores) - (t_pos - teach_cols)
    slopes_cols = coef * (hit.astype(jnp.float32) * total - errors)

    slopes = [
        lax.all_gather(slopes_cols[:, k * sub : (k + 1) * sub], "width", axis=1, tiled=True)
        for k in range(STEPS)
    ]

    query_wide = queries.astype(jnp.float32)
    grad_q = None
    terms = []
    for k in range(STEPS):
        block_slopes = slopes[k]
        gq = wide_dot(block_slopes, held[k].astype(jnp.float32))
        grad_q = gq if grad_q is None else grad_q + gq
        terms.append(wide_dot(block_slopes.T, query_wide))
    grad_p = terms[STEPS - 1]
    for k in range(STEPS - 2, -1, -1):
        grad_p = shifted(grad_p, "loop", -1) + terms[k]
    return (grad_q, grad_p)


def solution(mesh):
    in_specs = (P("loop", "width"), P("loop", "width"), P("loop", None), P("loop"))
    out_specs = (P("loop", "width"), P("loop", "width"))
    return jax.shard_map(
        per_device, mesh=mesh, in_specs=in_specs, out_specs=out_specs, check_vma=False
    )
```

```python
import jax
import jax.numpy as jnp
from jax import lax
from jax.sharding import PartitionSpec as P

STEPS = 4


SCALE = 20.0


def shifted(block, axis, distance):
    devices = range(lax.axis_size(axis))
    route = [((i - distance) % len(devices), i) for i in devices]
    return lax.ppermute(block, axis, route)


def wide_dot(a, b):
    return jnp.dot(a, b, precision=lax.Precision.HIGH, preferred_element_type=jnp.float32)


def per_device(queries, passages, teacher, positives):
    rows = queries.shape[0]
    width = lax.axis_size("width")
    me = lax.axis_index("width")
    sub = rows // width
    window = STEPS * rows

    q_full = lax.all_gather(queries, "width", axis=1, tiled=True)
    p_cols = lax.all_to_all(passages, "width", 0, 1, tiled=True)
    held_cols = [p_cols]
    held = [passages]
    for step in range(1, STEPS):
        held_cols.append(shifted(held_cols[-1], "loop", 1))
        held.append(shifted(held[-1], "loop", 1))

    cols = jnp.concatenate(held_cols, 0)
    raw = jnp.einsum("qd,cd->qc", q_full, cols, preferred_element_type=jnp.float32)
    gathered = [
        lax.all_gather(raw[:, k * sub : (k + 1) * sub], "width", axis=1, tiled=True)
        for k in range(STEPS)
    ]
    scores = SCALE * raw

    index = positives[:, None]
    teach = teacher.astype(jnp.float32)
    column = lax.broadcasted_iota(jnp.int32, teach.shape, 1)
    t_pos = jnp.sum(jnp.where(column == index, teach, 0.0), 1, keepdims=True)

    local = lax.broadcasted_iota(jnp.int32, (1, STEPS * sub), 1)
    wcol = (local // sub) * rows + me * sub + local % sub
    hit = wcol == index
    teach_cols = lax.dynamic_slice_in_dim(
        teach.reshape(rows, STEPS, width, sub), me, 1, 2
    ).reshape(rows, STEPS * sub)

    pos_part = jnp.sum(jnp.where(hit, scores, 0.0), 1)
    row_part = jnp.sum(scores, 1) - jnp.sum(teach_cols, 1)
    stats = lax.psum(jnp.stack([pos_part, row_part], 0), "width")
    s_pos = stats[0][:, None]
    total = window * (s_pos - t_pos) - stats[1][:, None]
    coef = SCALE * 2.0 / (window - 1)
    block_col = lax.broadcasted_iota(jnp.int32, (rows, rows), 1)

    query_wide = queries.astype(jnp.float32)
    grad_q = None
    terms = []
    for k in range(STEPS):
        block_scores = SCALE * gathered[k]
        errors = (s_pos - block_scores) - (t_pos - teach[:, k * rows : (k + 1) * rows])
        block_hit = (block_col + k * rows == index).astype(jnp.float32)
        block_slopes = coef * (block_hit * total - errors)
        gq = wide_dot(block_slopes, held[k].astype(jnp.float32))
        grad_q = gq if grad_q is None else grad_q + gq
        terms.append(wide_dot(block_slopes.T, query_wide))
    grad_p = terms[STEPS - 1]
    for k in range(STEPS - 2, -1, -1):
        grad_p = shifted(grad_p, "loop", -1) + terms[k]
    return (grad_q, grad_p)


def solution(mesh):
    in_specs = (P("loop", "width"), P("loop", "width"), P("loop", None), P("loop"))
    out_specs = (P("loop", "width"), P("loop", "width"))
    return jax.shard_map(
        per_device, mesh=mesh, in_specs=in_specs, out_specs=out_specs, check_vma=False
    )
```

```python
import jax
import jax.numpy as jnp
from jax import lax
from jax.sharding import PartitionSpec as P

STEPS = 4


SCALE = 20.0


def shifted(block, axis, distance):
    devices = range(lax.axis_size(axis))
    route = [((i - distance) % len(devices), i) for i in devices]
    return lax.ppermute(block, axis, route)


def after(value, dep):
    zero = 0.0 * dep[:1, :1]
    return value + zero.astype(value.dtype)


def wide_dot(a, b):
    return jnp.dot(a, b, precision=lax.Precision.HIGH, preferred_element_type=jnp.float32)


def per_device(queries, passages, teacher, positives):
    rows = queries.shape[0]
    width = lax.axis_size("width")
    me = lax.axis_index("width")
    sub = rows // width
    window = STEPS * rows

    q_full = lax.all_gather(queries, "width", axis=1, tiled=True)
    p_cols = lax.all_to_all(passages, "width", 0, 1, tiled=True)
    held_cols = [p_cols]
    held = [passages]
    for step in range(1, STEPS):
        held_cols.append(shifted(held_cols[-1], "loop", 1))
        held.append(shifted(held[-1], "loop", 1))

    cols = jnp.concatenate(held_cols, 0)
    raw = jnp.einsum("qd,cd->qc", q_full, cols, preferred_element_type=jnp.float32)
    gathered = [None] * STEPS
    for k in range(STEPS - 1, -1, -1):
        piece = raw[:, k * sub : (k + 1) * sub]
        if k < STEPS - 1:
            piece = after(piece, gathered[k + 1])
        gathered[k] = lax.all_gather(piece, "width", axis=1, tiled=True)
    scores = SCALE * raw

    index = positives[:, None]
    teach = teacher.astype(jnp.float32)
    column = lax.broadcasted_iota(jnp.int32, teach.shape, 1)
    t_pos = jnp.sum(jnp.where(column == index, teach, 0.0), 1, keepdims=True)

    local = lax.broadcasted_iota(jnp.int32, (1, STEPS * sub), 1)
    wcol = (local // sub) * rows + me * sub + local % sub
    hit = wcol == index
    teach_cols = lax.dynamic_slice_in_dim(
        teach.reshape(rows, STEPS, width, sub), me, 1, 2
    ).reshape(rows, STEPS * sub)

    pos_part = jnp.sum(jnp.where(hit, scores, 0.0), 1)
    row_part = jnp.sum(scores, 1) - jnp.sum(teach_cols, 1)
    stats = lax.psum(jnp.stack([pos_part, row_part], 0), "width")
    s_pos = stats[0][:, None]
    total = window * (s_pos - t_pos) - stats[1][:, None]
    coef = SCALE * 2.0 / (window - 1)
    block_col = lax.broadcasted_iota(jnp.int32, (rows, rows), 1)

    query_wide = queries.astype(jnp.float32)
    grad_q = None
    terms = []
    for k in range(STEPS):
        block_scores = SCALE * gathered[k]
        errors = (s_pos - block_scores) - (t_pos - teach[:, k * rows : (k + 1) * rows])
        block_hit = (block_col + k * rows == index).astype(jnp.float32)
        block_slopes = coef * (block_hit * total - errors)
        gq = wide_dot(block_slopes, held[k].astype(jnp.float32))
        grad_q = gq if grad_q is None else grad_q + gq
        terms.append(wide_dot(block_slopes.T, query_wide))
    grad_p = terms[STEPS - 1]
    for k in range(STEPS - 2, -1, -1):
        grad_p = shifted(grad_p, "loop", -1) + terms[k]
    return (grad_q, grad_p)


def solution(mesh):
    in_specs = (P("loop", "width"), P("loop", "width"), P("loop", None), P("loop"))
    out_specs = (P("loop", "width"), P("loop", "width"))
    return jax.shard_map(
        per_device, mesh=mesh, in_specs=in_specs, out_specs=out_specs, check_vma=False
    )
```

```python
import jax
import jax.numpy as jnp
from jax import lax
from jax.sharding import PartitionSpec as P

STEPS = 4


SCALE = 20.0


def shifted(block, axis, distance):
    devices = range(lax.axis_size(axis))
    route = [((i - distance) % len(devices), i) for i in devices]
    return lax.ppermute(block, axis, route)


def after(value, dep):
    zero = 0.0 * dep[:1, :1]
    return value + zero.astype(value.dtype)


def wide_dot(a, b):
    return jnp.dot(a, b, precision=lax.Precision.HIGH, preferred_element_type=jnp.float32)


def per_device(queries, passages, teacher, positives):
    rows = queries.shape[0]
    width = lax.axis_size("width")
    me = lax.axis_index("width")
    sub = rows // width
    window = STEPS * rows

    q_full = lax.all_gather(queries, "width", axis=1, tiled=True)
    p_cols = lax.all_to_all(passages, "width", 0, 1, tiled=True)
    held_cols = [p_cols]
    held = [passages]
    for step in range(1, STEPS):
        held_cols.append(shifted(held_cols[-1], "loop", 1))
        held.append(shifted(held[-1], "loop", 1))

    cols = after(jnp.concatenate(held_cols, 0), held[-1])
    raw = jnp.einsum("qd,cd->qc", q_full, cols, preferred_element_type=jnp.float32)
    gathered = [
        lax.all_gather(raw[:, k * sub : (k + 1) * sub], "width", axis=1, tiled=True)
        for k in range(STEPS)
    ]
    scores = SCALE * raw

    index = positives[:, None]
    teach = teacher.astype(jnp.float32)
    column = lax.broadcasted_iota(jnp.int32, teach.shape, 1)
    t_pos = jnp.sum(jnp.where(column == index, teach, 0.0), 1, keepdims=True)

    local = lax.broadcasted_iota(jnp.int32, (1, STEPS * sub), 1)
    wcol = (local // sub) * rows + me * sub + local % sub
    hit = wcol == index
    teach_cols = lax.dynamic_slice_in_dim(
        teach.reshape(rows, STEPS, width, sub), me, 1, 2
    ).reshape(rows, STEPS * sub)

    pos_part = jnp.sum(jnp.where(hit, scores, 0.0), 1)
    row_part = jnp.sum(scores, 1) - jnp.sum(teach_cols, 1)
    stats = lax.psum(jnp.stack([pos_part, row_part], 0), "width")
    s_pos = stats[0][:, None]
    total = window * (s_pos - t_pos) - stats[1][:, None]
    coef = SCALE * 2.0 / (window - 1)
    block_col = lax.broadcasted_iota(jnp.int32, (rows, rows), 1)

    query_wide = queries.astype(jnp.float32)
    grad_q = None
    terms = []
    for k in range(STEPS):
        block_scores = SCALE * gathered[k]
        errors = (s_pos - block_scores) - (t_pos - teach[:, k * rows : (k + 1) * rows])
        block_hit = (block_col + k * rows == index).astype(jnp.float32)
        block_slopes = coef * (block_hit * total - errors)
        gq = wide_dot(block_slopes, held[k].astype(jnp.float32))
        grad_q = gq if grad_q is None else grad_q + gq
        terms.append(wide_dot(block_slopes.T, query_wide))
    grad_p = terms[STEPS - 1]
    for k in range(STEPS - 2, -1, -1):
        grad_p = shifted(grad_p, "loop", -1) + terms[k]
    return (grad_q, grad_p)


def solution(mesh):
    in_specs = (P("loop", "width"), P("loop", "width"), P("loop", None), P("loop"))
    out_specs = (P("loop", "width"), P("loop", "width"))
    return jax.shard_map(
        per_device, mesh=mesh, in_specs=in_specs, out_specs=out_specs, check_vma=False
    )
```

```python
import jax
import jax.numpy as jnp
from jax import lax
from jax.sharding import PartitionSpec as P

STEPS = 4


SCALE = 20.0


def shifted(block, axis, distance):
    devices = range(lax.axis_size(axis))
    route = [((i - distance) % len(devices), i) for i in devices]
    return lax.ppermute(block, axis, route)


def wide_dot(a, b):
    return jnp.dot(a, b, precision=lax.Precision.HIGH, preferred_element_type=jnp.float32)


def per_device(queries, passages, teacher, positives):
    rows = queries.shape[0]
    width = lax.axis_size("width")
    me = lax.axis_index("width")
    sub = rows // width
    window = STEPS * rows

    q_full = lax.all_gather(queries, "width", axis=1, tiled=True)
    p_cols = lax.all_to_all(passages, "width", 0, 1, tiled=True)
    held_cols = [p_cols]
    held = [passages]
    for step in range(1, STEPS):
        held_cols.append(shifted(held_cols[-1], "loop", 1))
        held.append(shifted(held[-1], "loop", 1))

    cols = jnp.concatenate(held_cols, 0)
    raw = jnp.einsum("qd,cd->qc", q_full, cols, preferred_element_type=jnp.float32)
    gathered = [
        lax.all_gather(raw[:, k * sub : (k + 1) * sub], "width", axis=1, tiled=True)
        for k in range(STEPS)
    ]
    scores = SCALE * raw

    index = positives[:, None]
    column = lax.broadcasted_iota(jnp.int32, teacher.shape, 1)
    t_pos = jnp.sum(
        jnp.where(column == index, teacher.astype(jnp.float32), 0.0), 1, keepdims=True
    )

    local = lax.broadcasted_iota(jnp.int32, (1, STEPS * sub), 1)
    wcol = (local // sub) * rows + me * sub + local % sub
    hit = wcol == index
    teach_cols = lax.dynamic_slice_in_dim(
        teacher.reshape(rows, STEPS, width, sub), me, 1, 2
    ).reshape(rows, STEPS * sub).astype(jnp.float32)

    pos_part = jnp.sum(jnp.where(hit, scores, 0.0), 1)
    row_part = jnp.sum(scores, 1) - jnp.sum(teach_cols, 1)
    stats = lax.psum(jnp.stack([pos_part, row_part], 0), "width")
    s_pos = stats[0][:, None]
    total = window * (s_pos - t_pos) - stats[1][:, None]
    coef = SCALE * 2.0 / (window - 1)
    block_col = lax.broadcasted_iota(jnp.int32, (rows, rows), 1)

    query_wide = queries.astype(jnp.float32)
    grad_q = None
    terms = []
    for k in range(STEPS):
        block_scores = SCALE * gathered[k]
        errors = (s_pos - block_scores) - (t_pos - teacher[:, k * rows : (k + 1) * rows].astype(jnp.float32))
        block_hit = (block_col + k * rows == index).astype(jnp.float32)
        block_slopes = coef * (block_hit * total - errors)
        gq = wide_dot(block_slopes, held[k].astype(jnp.float32))
        grad_q = gq if grad_q is None else grad_q + gq
        terms.append(wide_dot(block_slopes.T, query_wide))
    grad_p = terms[STEPS - 1]
    for k in range(STEPS - 2, -1, -1):
        grad_p = shifted(grad_p, "loop", -1) + terms[k]
    return (grad_q, grad_p)


def solution(mesh):
    in_specs = (P("loop", "width"), P("loop", "width"), P("loop", None), P("loop"))
    out_specs = (P("loop", "width"), P("loop", "width"))
    return jax.shard_map(
        per_device, mesh=mesh, in_specs=in_specs, out_specs=out_specs, check_vma=False
    )
```
